256 devices in a mesh: tensor: 2 (over core), row: 16 (over x, y), col: 8 (over z).
Axes of the slice: x: 4, y: 4, z: 8, core: 2. Of those that a mesh axis runs over, the one named last changes fastest.
Arguments:
- integral_tiles: bfloat16 [8192, 8, 4096], P(('tensor', 'row', 'col')), may hold values from -6 to 6
- tile_index: int32 [8192, 3], P(('tensor', 'row', 'col')), may hold values from 0 to 127, as said below
- virtual_coeff: bfloat16 [8192, 2048], P('col'), may hold values from -0.09375 to 0.09375
- occupied_coeff: bfloat16 [2048, 512], P('row'), may hold values from -0.125 to 0.125
Outputs:
- pair_tensor: bfloat16 [2048, 32, 512], P(('row', 'col'), 'tensor')
The draws below stay inside these ranges and needn't reach their ends.
Inputs may be any that keep to these rules, and one draw needn't show every extreme that they name: `tile_index`: the tiles of the device at index (t, r, c) of tensor, row, col all have their nu block in c * 16 .. (c + 1) * 16 - 1, their auxiliary block below 4 and their mu block below 32. A tile's owner is (tensor index a // 2, row index m // 2) in the same col. Each device holds at most 2 tiles for any one owner; in every draw some owner gets exactly 2 tiles from every device of its col. Tiles with equal indices may occur and add up.
All inputs are finite; a program needn't handle non-finite values.
Results may differ from the reference program's by a relative error of at most 0.025.
Values may be sent and summed in bfloat16 or wider, within the bound.
No kernel may reach another device: no remote copies, remote signals or barrier semaphores. Data moves between devices by JAX's collectives and lax.ppermute only.
A program may use at most 128 MiB of HBM per device.

```python
import jax
import jax.numpy as jnp
from jax import lax

TB = 64
PB = 8
AB = 2
MB = 2
NBC = 16
CAP = 2
NV = 2048
NOCC = 512
K_DEV = 32
NMU = 32
NNU = 128
TILES = 8192
N_TENSOR = 2
N_ROW = 16
N_COL = 8


def draw_tile_index(key, part):
    owners = N_TENSOR * N_ROW
    sources = N_TENSOR * N_ROW * N_COL
    hot_count = owners // 4
    order = jax.random.permutation(jax.random.fold_in(key, 11), owners)
    hot_slots = jnp.repeat(order[:hot_count], CAP)
    cold_slots = jnp.repeat(order[hot_count:], CAP)
    half_held = K_DEV // 2

    def one_device(device_key):
        picked = jax.random.permutation(jax.random.fold_in(device_key, 1), cold_slots.shape[0])[:half_held]
        target = jnp.concatenate([hot_slots, cold_slots[picked]])
        target = target[jax.random.permutation(jax.random.fold_in(device_key, 2), K_DEV)]
        aux_local = jax.random.randint(jax.random.fold_in(device_key, 3), (K_DEV,), 0, AB)
        mu_local = jax.random.randint(jax.random.fold_in(device_key, 4), (K_DEV,), 0, MB)
        nu_local = jax.random.randint(jax.random.fold_in(device_key, 5), (K_DEV,), 0, NBC)
        nu_local = nu_local.at[0].set(NBC - 1).at[1].set(0)
        return (target, aux_local, mu_local, nu_local)
    device_keys = jax.random.split(jax.random.fold_in(key, 13), sources)
    target, aux_local, mu_local, nu_local = jax.vmap(one_device)(device_keys)
    column = (jnp.arange(sources, dtype=jnp.int32) % N_COL)[:, None]
    aux_block = target // N_ROW * AB + aux_local
    mu_block = target % N_ROW * MB + mu_local
    nu_block = column * NBC + nu_local
    stacked = jnp.stack([aux_block, mu_block, nu_block], axis=-1)
    return stacked.reshape(sources * K_DEV, 3).astype(jnp.int32)


def spiked(array, stream_key, source, target, parts, factor):
    owner, partner = [(jnp.arange(array.shape[position]) // (array.shape[position] // parts)).reshape([-1 if axis == position else 1 for axis in range(array.ndim)]) for position in (source, target)]
    chosen = jax.random.permutation(stream_key, parts)[partner]
    strong = (owner == chosen) | (owner == (partner + parts // 2) % parts)
    return jnp.where(strong, factor * array, array)


def steps_of(own_key, extent, shards, smallest, largest):
    loudness, own = 1.0, jax.random.fold_in(own_key, 6)
    for axis_at, blocks in shards:
        heights = jnp.exp(jax.random.uniform(jax.random.fold_in(own, axis_at), (blocks,), jnp.float32, smallest / len(shards), largest / len(shards)))
        loudness = loudness * jnp.repeat(heights, extent[axis_at] // blocks).reshape([-1 if axis == axis_at else 1 for axis in range(len(extent))])
    return loudness


def normal_values(stream_key, dims, deviation, bound, cuts=(), kind=jnp.bfloat16):
    array = jax.random.normal(stream_key, dims, jnp.float32) * deviation
    if len(cuts) > 0:
        array = steps_of(stream_key, dims, cuts, -0.22, 0.18) * array
    return jnp.clip(array, min=-bound, max=bound).astype(kind)


def bell_draw_with(key, dims, deviation, most, cuts, heavy, held_as=jnp.bfloat16):
    values = deviation * jax.random.normal(key, dims, jnp.float32)
    if cuts:
        values = values * steps_of(key, dims, cuts, -0.22, 0.18)
    return jnp.clip(spiked(values, jax.random.fold_in(key, 3), *heavy), -most, most).astype(held_as)


def setup_inputs(seed: int = 0) -> dict:
    keys = jax.random.split(jax.random.key(seed), 5)
    integral_tiles = normal_values(keys[0], (TILES, PB, TB * TB), 1.0, 6.0, ((0, 256),))
    tile_index = draw_tile_index(jax.random.fold_in(keys[4], 71), 0)
    virtual_coeff = bell_draw_with(keys[2], (NNU * TB, NV), (NNU * TB) ** -0.5, 0.09375, ((0, 8),), (0, 1, 8, 2.0))
    occupied_coeff = normal_values(keys[3], (NMU * TB, NOCC), (NMU * TB) ** -0.5, 0.125, ((0, 16),))
    return dict(integral_tiles=integral_tiles, tile_index=tile_index, virtual_coeff=virtual_coeff, occupied_coeff=occupied_coeff)


def reference(integral_tiles, tile_index, virtual_coeff, occupied_coeff):
    groups = N_TENSOR * N_ROW
    held = integral_tiles.shape[0] // (groups * N_COL)
    tile_len = PB * TB * TB
    by_column = jnp.moveaxis(integral_tiles.reshape(groups, N_COL, held, tile_len), 1, 0).reshape(N_COL, groups * held, tile_len)
    index_cols = jnp.moveaxis(tile_index.reshape(groups, N_COL, held, 3), 1, 0).reshape(N_COL, groups * held, 3)
    coeff_cols = virtual_coeff.reshape(N_COL, NBC, TB, NV)
    aux_blocks = N_TENSOR * AB
    mu_blocks = N_ROW * MB
    segments = aux_blocks * mu_blocks * NBC

    def add_column(total, pieces):
        tiles, index, coeff, column = pieces
        segment = (index[:, 0] * mu_blocks + index[:, 1]) * NBC + index[:, 2] - column * NBC
        dense = jax.ops.segment_sum(tiles.astype(jnp.float32), segment.astype(jnp.int32), num_segments=segments)
        dense = dense.astype(jnp.bfloat16).reshape(aux_blocks, mu_blocks, NBC, PB, TB, TB)
        part = jnp.einsum("knv,amkpun->vampu", coeff.astype(jnp.float32), dense.astype(jnp.float32))
        part = lax.optimization_barrier(part.astype(jnp.bfloat16))
        return total + part.astype(jnp.float32), None

    start_total = jnp.zeros((NV, aux_blocks, mu_blocks, PB, TB), jnp.float32)
    columns = jnp.arange(N_COL, dtype=jnp.int32)
    total, unused = lax.scan(add_column, start_total, (by_column, index_cols, coeff_cols, columns))
    half = total.astype(jnp.bfloat16)
    occupied = occupied_coeff.reshape(mu_blocks, TB, NOCC).astype(jnp.float32)
    result = jnp.einsum("vampu,muo->vapo", half.astype(jnp.float32), occupied)
    return result.reshape(NV, aux_blocks * PB, NOCC).astype(jnp.bfloat16)
```

```python
import jax
import jax.numpy as jnp
from jax import lax
from jax.sharding import PartitionSpec as P

TB = 64
PB = 8
AB = 2
MB = 2
NBC = 16
CAP = 2
NV = 2048
NOCC = 512


def shards(integral_tiles, tile_index, virtual_coeff, occupied_coeff):
    tensor_at = lax.axis_index("tensor")
    row_at = lax.axis_index("row")
    col_at = lax.axis_index("col")
    tensor_count = lax.axis_size("tensor")
    row_count = lax.axis_size("row")
    col_count = lax.axis_size("col")
    held = integral_tiles.shape[0]
    aux_blocks = tensor_count * AB
    mu_blocks = row_count * MB
    quarters = tensor_count * 2
    qsize = TB // quarters
    assert row_count == 2 * PB and quarters * qsize == TB

    tiles = integral_tiles.reshape(held, PB, 2, tensor_count, qsize, TB)
    send = tiles.transpose(3, 1, 2, 0, 4, 5).reshape(tensor_count * row_count, held, qsize * TB)
    recv = lax.all_to_all(send, ("tensor", "row"), split_axis=0, concat_axis=0, tiled=True)
    recv = recv.reshape(tensor_count * row_count * held, qsize * TB)
    index = lax.all_gather(tile_index, ("tensor", "row"), axis=0, tiled=True)

    local_nu = index[:, 2] - col_at * NBC
    block = (index[:, 0] * NBC + local_nu) * mu_blocks + index[:, 1]
    blocks = aux_blocks * NBC * mu_blocks
    selector = (jnp.arange(blocks)[:, None] == block[None, :]).astype(jnp.bfloat16)
    dense = jnp.dot(selector, recv, preferred_element_type=jnp.float32).astype(jnp.bfloat16)
    dense = dense.reshape(aux_blocks, NBC, mu_blocks, qsize, TB)

    occ_all = lax.all_gather(occupied_coeff, "row", axis=0, tiled=True)
    quarter = 2 * (row_at % 2) + tensor_at
    occ_q = lax.dynamic_index_in_dim(
        occ_all.reshape(mu_blocks, quarters, qsize, NOCC), quarter, axis=1, keepdims=False
    )
    partial = jnp.einsum("anmuw,mui->anwi", dense, occ_q, preferred_element_type=jnp.float32)

    pair = lax.psum_scatter(partial.astype(jnp.bfloat16), "tensor", scatter_dimension=0, tiled=True)
    side = row_at % 2
    keep = lax.dynamic_index_in_dim(pair, side, axis=0, keepdims=False)
    give = lax.dynamic_index_in_dim(pair, 1 - side, axis=0, keepdims=False)
    got = lax.ppermute(give, "row", perm=[(i, i ^ 1) for i in range(row_count)])
    occ_done = (keep.astype(jnp.float32) + got.astype(jnp.float32)).astype(jnp.bfloat16)

    chunk = NV // (row_count * col_count)
    virt = virtual_coeff.reshape(NBC, TB, row_count, col_count, chunk)
    z = jnp.einsum("nwi,nwrcj->crji", occ_done, virt, preferred_element_type=jnp.float32)
    z = z.astype(jnp.bfloat16).reshape(col_count * row_count * chunk, NOCC)
    w = lax.psum_scatter(z, "col", scatter_dimension=0, tiled=True).reshape(row_count, chunk, NOCC)

    got_rows = lax.all_to_all(w, "row", split_axis=0, concat_axis=0, tiled=True)
    out = got_rows.reshape(PB, 2, chunk, NOCC).transpose(2, 1, 0, 3)
    return out.reshape(chunk, AB * PB, NOCC)


def solution(mesh):
    in_specs = (
        P(("tensor", "row", "col"), None, None),
        P(("tensor", "row", "col"), None),
        P("col", None),
        P("row", None),
    )
    out_specs = P(("row", "col"), "tensor", None)
    return jax.shard_map(shards, mesh=mesh, in_specs=in_specs, out_specs=out_specs, check_vma=False)
```

```python
import jax
import jax.numpy as jnp
from jax import lax
from jax.sharding import PartitionSpec as P

TB = 64
PB = 8
AB = 2
MB = 2
NBC = 16
CAP = 2
NV = 2048
NOCC = 512


def shards(integral_tiles, tile_index, virtual_coeff, occupied_coeff):
    tensor_at = lax.axis_index("tensor")
    row_at = lax.axis_index("row")
    col_at = lax.axis_index("col")
    tensor_count = lax.axis_size("tensor")
    row_count = lax.axis_size("row")
    col_count = lax.axis_size("col")
    held = integral_tiles.shape[0]
    aux_blocks = tensor_count * AB
    mu_blocks = row_count * MB
    quarters = tensor_count * 2
    qsize = TB // quarters
    assert row_count == 2 * PB and quarters * qsize == TB

    owners = ("row", "tensor")
    send = integral_tiles.reshape(held, row_count * tensor_count, qsize * TB).transpose(1, 0, 2)
    recv = lax.all_to_all(send, owners, split_axis=0, concat_axis=0, tiled=True)
    recv = recv.reshape(tensor_count * row_count * held, qsize * TB)

    local_nu = tile_index[:, 2] - col_at * NBC
    own_block = (tile_index[:, 0] * NBC + local_nu) * mu_blocks + tile_index[:, 1]
    send_block = jnp.broadcast_to(own_block[None, :], (row_count * tensor_count, held))
    block = lax.all_to_all(send_block, owners, split_axis=0, concat_axis=0, tiled=True).reshape(-1)
    blocks = aux_blocks * NBC * mu_blocks
    selector = (jnp.arange(blocks)[:, None] == block[None, :]).astype(jnp.bfloat16)
    dense = jnp.dot(selector, recv, preferred_element_type=jnp.float32).astype(jnp.bfloat16)
    dense = dense.reshape(aux_blocks, NBC, mu_blocks, qsize, TB)

    occ_all = lax.all_gather(occupied_coeff, "row", axis=0, tiled=True)
    quarter = 2 * (row_at % 2) + tensor_at
    occ_q = lax.dynamic_index_in_dim(
        occ_all.reshape(mu_blocks, quarters, qsize, NOCC), quarter, axis=1, keepdims=False
    )
    partial = jnp.einsum("anmuw,mui->anwi", dense, occ_q, preferred_element_type=jnp.float32)

    pair = lax.psum_scatter(partial.astype(jnp.bfloat16), "tensor", scatter_dimension=0, tiled=True)
    side = row_at % 2
    keep = lax.dynamic_index_in_dim(pair, side, axis=0, keepdims=False)
    give = lax.dynamic_index_in_dim(pair, 1 - side, axis=0, keepdims=False)
    got = lax.ppermute(give, "row", perm=[(i, i ^ 1) for i in range(row_count)])
    occ_done = (keep.astype(jnp.float32) + got.astype(jnp.float32)).astype(jnp.bfloat16)

    chunk = NV // (row_count * col_count)
    virt = virtual_coeff.reshape(NBC, TB, NV)
    z = jnp.einsum("nwi,nwv->vi", occ_done, virt, preferred_element_type=jnp.float32).astype(jnp.bfloat16)
    z = z.reshape(row_count, col_count, chunk, NOCC).transpose(1, 0, 2, 3)
    z = z.reshape(col_count * row_count * chunk, NOCC)
    w = lax.psum_scatter(z, "col", scatter_dimension=0, tiled=True).reshape(row_count, chunk, NOCC)

    got_rows = lax.all_to_all(w, "row", split_axis=0, concat_axis=0, tiled=True)
    out = got_rows.reshape(PB, 2, chunk, NOCC).transpose(2, 1, 0, 3)
    return out.reshape(chunk, AB * PB, NOCC)


def solution(mesh):
    in_specs = (
        P(("tensor", "row", "col"), None, None),
        P(("tensor", "row", "col"), None),
        P("col", None),
        P("row", None),
    )
    out_specs = P(("row", "col"), "tensor", None)
    return jax.shard_map(shards, mesh=mesh, in_specs=in_specs, out_specs=out_specs, check_vma=False)
```

```python
import jax
import jax.numpy as jnp
from jax import lax
from jax.sharding import PartitionSpec as P

TB = 64
PB = 8
AB = 2
MB = 2
NBC = 16
CAP = 2
NV = 2048
NOCC = 512


def shards(integral_tiles, tile_index, virtual_coeff, occupied_coeff):
    tensor_at = lax.axis_index("tensor")
    row_at = lax.axis_index("row")
    col_at = lax.axis_index("col")
    tensor_count = lax.axis_size("tensor")
    row_count = lax.axis_size("row")
    col_count = lax.axis_size("col")
    held = integral_tiles.shape[0]
    aux_blocks = tensor_count * AB
    mu_blocks = row_count * MB
    quarters = tensor_count * 2
    qsize = TB // quarters
    assert row_count == 2 * PB and quarters * qsize == TB

    owners = ("row", "tensor")
    dests = row_count * tensor_count
    lanes = qsize * TB
    send = integral_tiles.reshape(held, dests, lanes).transpose(1, 0, 2)
    local_index = jnp.stack(
        [tile_index[:, 0], tile_index[:, 1], tile_index[:, 2] - col_at * NBC], axis=1
    ).astype(jnp.bfloat16).reshape(1, 1, held * 3)
    index_row = jnp.pad(local_index, ((0, 0), (0, 0), (0, lanes - held * 3)))
    send = jnp.concatenate([send, jnp.broadcast_to(index_row, (dests, 1, lanes))], axis=1)
    recv = lax.all_to_all(send, owners, split_axis=0, concat_axis=0, tiled=True)
    slices = recv[:, :held, :].reshape(dests * held, lanes)
    index = recv[:, held, : held * 3].astype(jnp.int32).reshape(dests * held, 3)

    block = (index[:, 0] * NBC + index[:, 2]) * mu_blocks + index[:, 1]
    blocks = aux_blocks * NBC * mu_blocks
    selector = (jnp.arange(blocks)[:, None] == block[None, :]).astype(jnp.bfloat16)
    dense = jnp.dot(selector, slices, preferred_element_type=jnp.float32).astype(jnp.bfloat16)
    dense = dense.reshape(aux_blocks * NBC, mu_blocks, qsize, TB).transpose(0, 3, 1, 2)
    dense = dense.reshape(aux_blocks * NBC, TB, mu_blocks * qsize)

    occ_local = occupied_coeff.reshape(MB, 2, tensor_count, qsize, NOCC)
    occ_local = lax.dynamic_index_in_dim(occ_local, tensor_at, axis=2, keepdims=False)
    occ_half = lax.all_gather(occ_local, "row", axis=0, tiled=True)
    occ_q = lax.dynamic_index_in_dim(occ_half, row_at % 2, axis=1, keepdims=False)
    occ_q = occ_q.reshape(mu_blocks * qsize, NOCC)
    partial = jnp.einsum("bwk,ki->bwi", dense, occ_q, preferred_element_type=jnp.float32)
    partial = partial.reshape(aux_blocks, NBC, TB, NOCC)

    pair = lax.psum_scatter(partial.astype(jnp.bfloat16), "tensor", scatter_dimension=0, tiled=True)
    side = row_at % 2
    keep = lax.dynamic_index_in_dim(pair, side, axis=0, keepdims=False)
    give = lax.dynamic_index_in_dim(pair, 1 - side, axis=0, keepdims=False)
    got = lax.ppermute(give, "row", perm=[(i, i ^ 1) for i in range(row_count)])
    occ_done = (keep.astype(jnp.float32) + got.astype(jnp.float32)).astype(jnp.bfloat16)

    chunk = NV // (row_count * col_count)
    virt = virtual_coeff.reshape(NBC, TB, NV)
    z = jnp.einsum("nwi,nwv->vi", occ_done, virt, preferred_element_type=jnp.float32).astype(jnp.bfloat16)
    z = z.reshape(row_count, col_count, chunk, NOCC).transpose(1, 0, 2, 3)
    z = z.reshape(col_count * row_count * chunk, NOCC)
    w = lax.psum_scatter(z, "col", scatter_dimension=0, tiled=True).reshape(row_count, chunk, NOCC)

    got_rows = lax.all_to_all(w, "row", split_axis=0, concat_axis=0, tiled=True)
    out = got_rows.reshape(PB, 2, chunk, NOCC).transpose(2, 1, 0, 3)
    return out.reshape(chunk, AB * PB, NOCC)


def solution(mesh):
    in_specs = (
        P(("tensor", "row", "col"), None, None),
        P(("tensor", "row", "col"), None),
        P("col", None),
        P("row", None),
    )
    out_specs = P(("row", "col"), "tensor", None)
    return jax.shard_map(shards, mesh=mesh, in_specs=in_specs, out_specs=out_specs, check_vma=False)
```

```python
import jax
import jax.numpy as jnp
from jax import lax
from jax.sharding import PartitionSpec as P

TB = 64
PB = 8
AB = 2
MB = 2
NBC = 16
CAP = 2
NV = 2048
NOCC = 512


def shards(integral_tiles, tile_index, virtual_coeff, occupied_coeff):
    tensor_at = lax.axis_index("tensor")
    row_at = lax.axis_index("row")
    col_at = lax.axis_index("col")
    tensor_count = lax.axis_size("tensor")
    row_count = lax.axis_size("row")
    col_count = lax.axis_size("col")
    held = integral_tiles.shape[0]
    aux_blocks = tensor_count * AB
    mu_blocks = row_count * MB
    quarters = tensor_count * 2
    qsize = TB // quarters
    assert row_count == 2 * PB and quarters * qsize == TB and row_count * tensor_count == mu_blocks

    owners = ("row", "tensor")
    dests = row_count * tensor_count
    lanes = qsize * TB
    send = integral_tiles.reshape(held, dests, lanes).transpose(1, 0, 2)
    local_index = jnp.stack(
        [tile_index[:, 0], tile_index[:, 1], tile_index[:, 2] - col_at * NBC], axis=1
    ).astype(jnp.bfloat16).reshape(1, 1, held * 3)
    index_row = jnp.pad(local_index, ((0, 0), (0, 0), (0, lanes - held * 3)))
    occ_rows = qsize * NOCC // lanes
    occ_block = lax.dynamic_index_in_dim(occupied_coeff.reshape(MB, TB, NOCC), tensor_at, 0, keepdims=False)
    occ_send = jnp.broadcast_to(occ_block.reshape(1, quarters, occ_rows, lanes), (PB, quarters, occ_rows, lanes))
    send = jnp.concatenate(
        [send, jnp.broadcast_to(index_row, (dests, 1, lanes)), occ_send.reshape(dests, occ_rows, lanes)], axis=1
    )
    recv = lax.all_to_all(send, owners, split_axis=0, concat_axis=0, tiled=True)
    slices = recv[:, :held, :].reshape(dests * held, lanes)
    index = recv[:, held, : held * 3].astype(jnp.int32).reshape(dests * held, 3)
    occ_q = recv[:, held + 1 :, :].reshape(mu_blocks * qsize, NOCC)

    block = (index[:, 0] * NBC + index[:, 2]) * mu_blocks + index[:, 1]
    blocks = aux_blocks * NBC * mu_blocks
    selector = (jnp.arange(blocks)[:, None] == block[None, :]).astype(jnp.bfloat16)
    dense = jnp.dot(selector, slices, preferred_element_type=jnp.float32).astype(jnp.bfloat16)
    dense = dense.reshape(aux_blocks * NBC, mu_blocks, qsize, TB).transpose(0, 3, 1, 2)
    dense = dense.reshape(aux_blocks * NBC, TB, mu_blocks * qsize)

    partial = jnp.einsum("bwk,ki->bwi", dense, occ_q, preferred_element_type=jnp.float32)
    partial = partial.reshape(aux_blocks, NBC, TB, NOCC)

    pair = lax.psum_scatter(partial.astype(jnp.bfloat16), "tensor", scatter_dimension=0, tiled=True)
    side = row_at % 2
    keep = lax.dynamic_index_in_dim(pair, side, axis=0, keepdims=False)
    give = lax.dynamic_index_in_dim(pair, 1 - side, axis=0, keepdims=False)
    got = lax.ppermute(give, "row", perm=[(i, i ^ 1) for i in range(row_count)])
    occ_done = (keep.astype(jnp.float32) + got.astype(jnp.float32)).astype(jnp.bfloat16)

    chunk = NV // (row_count * col_count)
    virt = virtual_coeff.reshape(NBC, TB, NV)
    z = jnp.einsum("nwi,nwv->vi", occ_done, virt, preferred_element_type=jnp.float32).astype(jnp.bfloat16)
    z = z.reshape(row_count, col_count, chunk, NOCC).transpose(1, 0, 2, 3)
    z = z.reshape(col_count * row_count * chunk, NOCC)
    w = lax.psum_scatter(z, "col", scatter_dimension=0, tiled=True).reshape(row_count, chunk, NOCC)

    got_rows = lax.all_to_all(w, "row", split_axis=0, concat_axis=0, tiled=True)
    out = got_rows.reshape(PB, 2, chunk, NOCC).transpose(2, 1, 0, 3)
    return out.reshape(chunk, AB * PB, NOCC)


def solution(mesh):
    in_specs = (
        P(("tensor", "row", "col"), None, None),
        P(("tensor", "row", "col"), None),
        P("col", None),
        P("row", None),
    )
    out_specs = P(("row", "col"), "tensor", None)
    return jax.shard_map(shards, mesh=mesh, in_specs=in_specs, out_specs=out_specs, check_vma=False)
```

```python
import jax
import jax.numpy as jnp
from jax import lax
from jax.sharding import PartitionSpec as P

TB = 64
PB = 8
AB = 2
MB = 2
NBC = 16
CAP = 2
NV = 2048
NOCC = 512


def shards(integral_tiles, tile_index, virtual_coeff, occupied_coeff):
    tensor_at = lax.axis_index("tensor")
    row_at = lax.axis_index("row")
    col_at = lax.axis_index("col")
    tensor_count = lax.axis_size("tensor")
    row_count = lax.axis_size("row")
    col_count = lax.axis_size("col")
    held = integral_tiles.shape[0]
    aux_blocks = tensor_count * AB
    mu_blocks = row_count * MB
    quarters = tensor_count * 2
    qsize = TB // quarters
    assert row_count == 2 * PB and tensor_count == 2 and quarters * qsize == TB

    owners = ("row", "tensor")
    dests = row_count * tensor_count
    lanes = qsize * TB
    send = integral_tiles.reshape(held, dests, lanes).transpose(1, 0, 2)
    local_index = jnp.stack(
        [tile_index[:, 0], tile_index[:, 1], tile_index[:, 2] - col_at * NBC], axis=1
    ).astype(jnp.bfloat16).reshape(1, 1, held * 3)
    index_row = jnp.pad(local_index, ((0, 0), (0, 0), (0, lanes - held * 3)))
    send = jnp.concatenate([send, jnp.broadcast_to(index_row, (dests, 1, lanes))], axis=1)
    recv = lax.all_to_all(send, owners, split_axis=0, concat_axis=0, tiled=True)
    slices = recv[:, :held, :].reshape(dests * held, lanes)
    index = recv[:, held, : held * 3].astype(jnp.int32).reshape(dests * held, 3)

    occ_all = lax.all_gather(occupied_coeff, "row", axis=0, tiled=True)
    quarter = 2 * (row_at % 2) + tensor_at
    occ_q = lax.dynamic_index_in_dim(
        occ_all.reshape(mu_blocks, quarters, qsize, NOCC), quarter, axis=1, keepdims=False
    ).reshape(mu_blocks * qsize, NOCC)

    block = (index[:, 0] * NBC + index[:, 2]) * mu_blocks + index[:, 1]
    blocks = aux_blocks * NBC * mu_blocks
    selector = (jnp.arange(blocks)[:, None] == block[None, :]).astype(jnp.bfloat16)
    dense = jnp.dot(selector, slices, preferred_element_type=jnp.float32).astype(jnp.bfloat16)
    dense = dense.reshape(aux_blocks * NBC, mu_blocks, qsize, TB).transpose(0, 3, 1, 2)
    dense = dense.reshape(aux_blocks * NBC, TB, mu_blocks * qsize)

    partial = jnp.einsum("bwk,ki->bwi", dense, occ_q, preferred_element_type=jnp.float32)
    partial = partial.reshape(aux_blocks, NBC, TB, NOCC)

    side = row_at % 2
    halves = []
    for half in jnp.split(partial.astype(jnp.bfloat16), 2, axis=3):
        pairs = half.reshape(tensor_count, AB, NBC, TB, NOCC // 2)
        mine = lax.dynamic_index_in_dim(pairs, tensor_at, axis=0, keepdims=False)
        other = lax.dynamic_index_in_dim(pairs, 1 - tensor_at, axis=0, keepdims=False)
        got_t = lax.ppermute(other, "tensor", perm=[(0, 1), (1, 0)])
        pair = (mine.astype(jnp.float32) + got_t.astype(jnp.float32)).astype(jnp.bfloat16)
        keep = lax.dynamic_index_in_dim(pair, side, axis=0, keepdims=False)
        give = lax.dynamic_index_in_dim(pair, 1 - side, axis=0, keepdims=False)
        got_r = lax.ppermute(give, "row", perm=[(i, i ^ 1) for i in range(row_count)])
        halves.append(keep.astype(jnp.float32) + got_r.astype(jnp.float32))
    occ_done = jnp.concatenate(halves, axis=2).astype(jnp.bfloat16)

    chunk = NV // (row_count * col_count)
    virt = virtual_coeff.reshape(NBC, TB, NV)
    z = jnp.einsum("nwi,nwv->vi", occ_done, virt, preferred_element_type=jnp.float32).astype(jnp.bfloat16)
    z = z.reshape(row_count, col_count, chunk, NOCC).transpose(1, 0, 2, 3)
    z = z.reshape(col_count * row_count * chunk, NOCC)
    w = lax.psum_scatter(z, "col", scatter_dimension=0, tiled=True).reshape(row_count, chunk, NOCC)

    got_rows = lax.all_to_all(w, "row", split_axis=0, concat_axis=0, tiled=True)
    out = got_rows.reshape(PB, 2, chunk, NOCC).transpose(2, 1, 0, 3)
    return out.reshape(chunk, AB * PB, NOCC)


def solution(mesh):
    in_specs = (
        P(("tensor", "row", "col"), None, None),
        P(("tensor", "row", "col"), None),
        P("col", None),
        P("row", None),
    )
    out_specs = P(("row", "col"), "tensor", None)
    return jax.shard_map(shards, mesh=mesh, in_specs=in_specs, out_specs=out_specs, check_vma=False)
```

```python
import jax
import jax.numpy as jnp
from jax import lax
from jax.sharding import PartitionSpec as P

TB = 64
PB = 8
AB = 2
MB = 2
NBC = 16
CAP = 2
NV = 2048
NOCC = 512


def shards(integral_tiles, tile_index, virtual_coeff, occupied_coeff):
    tensor_at = lax.axis_index("tensor")
    row_at = lax.axis_index("row")
    col_at = lax.axis_index("col")
    tensor_count = lax.axis_size("tensor")
    row_count = lax.axis_size("row")
    col_count = lax.axis_size("col")
    held = integral_tiles.shape[0]
    aux_blocks = tensor_count * AB
    mu_blocks = row_count * MB
    quarters = tensor_count * 2
    qsize = TB // quarters
    assert row_count == 2 * PB and tensor_count == 2 and quarters * qsize == TB

    owners = ("row", "tensor")
    dests = row_count * tensor_count
    lanes = qsize * TB
    send = integral_tiles.reshape(held, dests, lanes).transpose(1, 0, 2)
    local_index = jnp.stack(
        [tile_index[:, 0], tile_index[:, 1], tile_index[:, 2] - col_at * NBC], axis=1
    ).astype(jnp.bfloat16).reshape(1, 1, held * 3)
    index_row = jnp.pad(local_index, ((0, 0), (0, 0), (0, lanes - held * 3)))
    send = jnp.concatenate([send, jnp.broadcast_to(index_row, (dests, 1, lanes))], axis=1)
    recv = lax.all_to_all(send, owners, split_axis=0, concat_axis=0, tiled=True)
    slices = recv[:, :held, :].reshape(dests * held, lanes)
    index = recv[:, held, : held * 3].astype(jnp.int32).reshape(dests * held, 3)

    occ_all = lax.all_gather(occupied_coeff, "row", axis=0, tiled=True)
    quarter = 2 * (row_at % 2) + tensor_at
    occ_q = lax.dynamic_index_in_dim(
        occ_all.reshape(mu_blocks, quarters, qsize, NOCC), quarter, axis=1, keepdims=False
    ).reshape(mu_blocks * qsize, NOCC)

    block = (index[:, 0] * NBC + index[:, 2]) * mu_blocks + index[:, 1]
    blocks = aux_blocks * NBC * mu_blocks
    selector = (jnp.arange(blocks)[:, None] == block[None, :]).astype(jnp.bfloat16)
    dense = jnp.dot(selector, slices, preferred_element_type=jnp.float32).astype(jnp.bfloat16)
    dense = dense.reshape(aux_blocks * NBC, mu_blocks, qsize, TB).transpose(0, 3, 1, 2)
    dense = dense.reshape(aux_blocks * NBC, TB, mu_blocks * qsize)

    partial = jnp.einsum("bwk,ki->bwi", dense, occ_q, preferred_element_type=jnp.float32)
    partial = partial.reshape(aux_blocks, NBC, TB, NOCC)

    side = row_at % 2
    halves = []
    for half in jnp.split(partial.astype(jnp.bfloat16), 2, axis=3):
        pairs = half.reshape(tensor_count, AB, NBC, TB, NOCC // 2)
        mine = lax.dynamic_index_in_dim(pairs, tensor_at, axis=0, keepdims=False)
        other = lax.dynamic_index_in_dim(pairs, 1 - tensor_at, axis=0, keepdims=False)
        got_t = lax.ppermute(other, "tensor", perm=[(0, 1), (1, 0)])
        pair = (mine.astype(jnp.float32) + got_t.astype(jnp.float32)).astype(jnp.bfloat16)
        keep = lax.dynamic_index_in_dim(pair, side, axis=0, keepdims=False)
        give = lax.dynamic_index_in_dim(pair, 1 - side, axis=0, keepdims=False)
        got_r = lax.ppermute(give, "row", perm=[(i, i ^ 1) for i in range(row_count)])
        halves.append(keep.astype(jnp.float32) + got_r.astype(jnp.float32))
    occ_done = jnp.concatenate(halves, axis=2).astype(jnp.bfloat16)

    chunk = NV // (row_count * col_count)
    virt = virtual_coeff.reshape(NBC, TB, NV)
    z = jnp.einsum("nwi,nwv->vi", occ_done, virt, preferred_element_type=jnp.float32).astype(jnp.bfloat16)
    z = z.reshape(row_count, col_count, chunk, NOCC).transpose(1, 0, 2, 3)
    z = z.reshape(col_count, row_count * chunk, NOCC)
    lanes_half = NOCC // 2
    ring = (z[:, :, :lanes_half], z[:, :, lanes_half:])
    steps = (1, -1)
    accs = [
        lax.dynamic_index_in_dim(part, (col_at - step) % col_count, axis=0, keepdims=False)
        for part, step in zip(ring, steps)
    ]
    for hop in range(col_count - 1):
        for which in range(2):
            step = steps[which]
            perm = [(i, (i + step) % col_count) for i in range(col_count)]
            got = lax.ppermute(accs[which], "col", perm=perm)
            own = lax.dynamic_index_in_dim(ring[which], (col_at - step * (hop + 2)) % col_count, axis=0, keepdims=False)
            accs[which] = (got.astype(jnp.float32) + own.astype(jnp.float32)).astype(jnp.bfloat16)
    w = jnp.concatenate(accs, axis=-1).reshape(row_count, chunk, NOCC)

    got_rows = lax.all_to_all(w, "row", split_axis=0, concat_axis=0, tiled=True)
    out = got_rows.reshape(PB, 2, chunk, NOCC).transpose(2, 1, 0, 3)
    return out.reshape(chunk, AB * PB, NOCC)


def solution(mesh):
    in_specs = (
        P(("tensor", "row", "col"), None, None),
        P(("tensor", "row", "col"), None),
        P("col", None),
        P("row", None),
    )
    out_specs = P(("row", "col"), "tensor", None)
    return jax.shard_map(shards, mesh=mesh, in_specs=in_specs, out_specs=out_specs, check_vma=False)
```

```python
import jax
import jax.numpy as jnp
from jax import lax
from jax.sharding import PartitionSpec as P

TB = 64
PB = 8
AB = 2
MB = 2
NBC = 16
CAP = 2
NV = 2048
NOCC = 512


def shards(integral_tiles, tile_index, virtual_coeff, occupied_coeff):
    tensor_at = lax.axis_index("tensor")
    row_at = lax.axis_index("row")
    col_at = lax.axis_index("col")
    tensor_count = lax.axis_size("tensor")
    row_count = lax.axis_size("row")
    col_count = lax.axis_size("col")
    held = integral_tiles.shape[0]
    aux_blocks = tensor_count * AB
    mu_blocks = row_count * MB
    quarters = tensor_count * 2
    qsize = TB // quarters
    assert row_count == 2 * PB and tensor_count == 2 and quarters * qsize == TB

    owners = ("row", "tensor")
    dests = row_count * tensor_count
    lanes = qsize * TB
    send = integral_tiles.reshape(held, dests, lanes).transpose(1, 0, 2)
    local_index = jnp.stack(
        [tile_index[:, 0], tile_index[:, 1], tile_index[:, 2] - col_at * NBC], axis=1
    ).astype(jnp.bfloat16).reshape(1, 1, held * 3)
    index_row = jnp.pad(local_index, ((0, 0), (0, 0), (0, lanes - held * 3)))
    send = jnp.concatenate([send, jnp.broadcast_to(index_row, (dests, 1, lanes))], axis=1)
    recv = lax.all_to_all(send, owners, split_axis=0, concat_axis=0, tiled=True)
    slices = recv[:, :held, :].reshape(dests * held, lanes)
    index = recv[:, held, : held * 3].astype(jnp.int32).reshape(dests * held, 3)

    occ_all = lax.all_gather(occupied_coeff, "row", axis=0, tiled=True)
    quarter = 2 * (row_at % 2) + tensor_at
    occ_q = lax.dynamic_index_in_dim(
        occ_all.reshape(mu_blocks, quarters, qsize, NOCC), quarter, axis=1, keepdims=False
    ).reshape(mu_blocks * qsize, NOCC)

    block = (index[:, 0] * NBC + index[:, 2]) * mu_blocks + index[:, 1]
    blocks = aux_blocks * NBC * mu_blocks
    selector = (jnp.arange(blocks)[:, None] == block[None, :]).astype(jnp.bfloat16)
    dense = jnp.dot(selector, slices, preferred_element_type=jnp.float32).astype(jnp.bfloat16)
    dense = dense.reshape(aux_blocks * NBC, mu_blocks, qsize, TB).transpose(0, 3, 1, 2)
    dense = dense.reshape(aux_blocks * NBC, TB, mu_blocks * qsize)

    partial = jnp.einsum("bwk,ki->bwi", dense, occ_q, preferred_element_type=jnp.float32)
    partial = partial.reshape(aux_blocks, NBC, TB, NOCC)

    side = row_at % 2
    halves = []
    for half in jnp.split(partial.astype(jnp.bfloat16), 2, axis=3):
        pairs = half.reshape(tensor_count, AB, NBC, TB, NOCC // 2)
        mine = lax.dynamic_index_in_dim(pairs, tensor_at, axis=0, keepdims=False)
        other = lax.dynamic_index_in_dim(pairs, 1 - tensor_at, axis=0, keepdims=False)
        got_t = lax.ppermute(other, "tensor", perm=[(0, 1), (1, 0)])
        pair = (mine.astype(jnp.float32) + got_t.astype(jnp.float32)).astype(jnp.bfloat16)
        keep = lax.dynamic_index_in_dim(pair, side, axis=0, keepdims=False)
        give = lax.dynamic_index_in_dim(pair, 1 - side, axis=0, keepdims=False)
        got_r = lax.ppermute(give, "row", perm=[(i, i ^ 1) for i in range(row_count)])
        halves.append(keep.astype(jnp.float32) + got_r.astype(jnp.float32))
    occ_done = jnp.concatenate(halves, axis=2).astype(jnp.bfloat16)

    chunk = NV // (row_count * col_count)
    virt = virtual_coeff.reshape(NBC, TB, NV)
    z = jnp.einsum("nwi,nwv->vi", occ_done, virt, preferred_element_type=jnp.float32).astype(jnp.bfloat16)
    z = z.reshape(row_count, col_count, chunk, NOCC).transpose(1, 0, 2, 3)
    z = z.reshape(col_count, row_count * chunk, NOCC)
    lanes_half = NOCC // 2
    native = lax.psum_scatter(
        z[:, :, :lanes_half].reshape(col_count * row_count * chunk, lanes_half), "col",
        scatter_dimension=0, tiled=True,
    )
    ring = z[:, :, lanes_half:]
    acc = lax.dynamic_index_in_dim(ring, (col_at + 1) % col_count, axis=0, keepdims=False)
    perm = [(i, (i - 1) % col_count) for i in range(col_count)]
    for hop in range(col_count - 1):
        got = lax.ppermute(acc, "col", perm=perm)
        own = lax.dynamic_index_in_dim(ring, (col_at + hop + 2) % col_count, axis=0, keepdims=False)
        acc = (got.astype(jnp.float32) + own.astype(jnp.float32)).astype(jnp.bfloat16)
    w = jnp.concatenate([native, acc], axis=-1).reshape(row_count, chunk, NOCC)

    got_rows = lax.all_to_all(w, "row", split_axis=0, concat_axis=0, tiled=True)
    out = got_rows.reshape(PB, 2, chunk, NOCC).transpose(2, 1, 0, 3)
    return out.reshape(chunk, AB * PB, NOCC)


def solution(mesh):
    in_specs = (
        P(("tensor", "row", "col"), None, None),
        P(("tensor", "row", "col"), None),
        P("col", None),
        P("row", None),
    )
    out_specs = P(("row", "col"), "tensor", None)
    return jax.shard_map(shards, mesh=mesh, in_specs=in_specs, out_specs=out_specs, check_vma=False)
```

```python
import jax
import jax.numpy as jnp
from jax import lax
from jax.sharding import PartitionSpec as P

TB = 64
PB = 8
AB = 2
MB = 2
NBC = 16
CAP = 2
NV = 2048
NOCC = 512


def shards(integral_tiles, tile_index, virtual_coeff, occupied_coeff):
    tensor_at = lax.axis_index("tensor")
    row_at = lax.axis_index("row")
    col_at = lax.axis_index("col")
    tensor_count = lax.axis_size("tensor")
    row_count = lax.axis_size("row")
    col_count = lax.axis_size("col")
    held = integral_tiles.shape[0]
    aux_blocks = tensor_count * AB
    mu_blocks = row_count * MB
    quarters = tensor_count * 2
    qsize = TB // quarters
    assert row_count == 2 * PB and tensor_count == 2 and quarters * qsize == TB

    owners = ("row", "tensor")
    dests = row_count * tensor_count
    lanes = qsize * TB
    send = integral_tiles.reshape(held, PB, quarters, lanes).transpose(1, 2, 0, 3).reshape(dests, held, lanes)
    local_index = jnp.stack(
        [tile_index[:, 0], tile_index[:, 1], tile_index[:, 2] - col_at * NBC], axis=1
    ).astype(jnp.bfloat16).reshape(1, 1, held * 3)
    index_row = jnp.pad(local_index, ((0, 0), (0, 0), (0, lanes - held * 3)))
    send = jnp.concatenate([send, jnp.broadcast_to(index_row, (dests, 1, lanes))], axis=1)
    recv = lax.all_to_all(send, owners, split_axis=0, concat_axis=0, tiled=True)
    slices = recv[:, :held, :].reshape(dests * held, lanes)
    index = recv[:, held, : held * 3].astype(jnp.int32).reshape(dests * held, 3)

    occ_all = lax.all_gather(occupied_coeff, "row", axis=0, tiled=True)
    quarter = 2 * (row_at % 2) + tensor_at
    occ_q = lax.dynamic_index_in_dim(
        occ_all.reshape(mu_blocks, quarters, qsize, NOCC), quarter, axis=1, keepdims=False
    ).reshape(mu_blocks * qsize, NOCC)

    block = (index[:, 0] * NBC + index[:, 2]) * mu_blocks + index[:, 1]
    blocks = aux_blocks * NBC * mu_blocks
    selector = (jnp.arange(blocks)[:, None] == block[None, :]).astype(jnp.bfloat16)
    dense = jnp.dot(selector, slices, preferred_element_type=jnp.float32).astype(jnp.bfloat16)
    dense = dense.reshape(aux_blocks * NBC, mu_blocks, qsize, TB).transpose(0, 3, 1, 2)
    dense = dense.reshape(aux_blocks * NBC, TB, mu_blocks * qsize)

    partial = jnp.einsum("bwk,ki->bwi", dense, occ_q, preferred_element_type=jnp.float32)
    partial = partial.reshape(aux_blocks, NBC, TB, NOCC)

    side = row_at % 2
    halves = []
    for half in jnp.split(partial.astype(jnp.bfloat16), 2, axis=3):
        pairs = half.reshape(tensor_count, AB, NBC, TB, NOCC // 2)
        mine = lax.dynamic_index_in_dim(pairs, tensor_at, axis=0, keepdims=False)
        other = lax.dynamic_index_in_dim(pairs, 1 - tensor_at, axis=0, keepdims=False)
        got_t = lax.ppermute(other, "tensor", perm=[(0, 1), (1, 0)])
        pair = (mine.astype(jnp.float32) + got_t.astype(jnp.float32)).astype(jnp.bfloat16)
        keep = lax.dynamic_index_in_dim(pair, side, axis=0, keepdims=False)
        give = lax.dynamic_index_in_dim(pair, 1 - side, axis=0, keepdims=False)
        got_r = lax.ppermute(give, "row", perm=[(i, i ^ 1) for i in range(row_count)])
        halves.append((keep.astype(jnp.float32) + got_r.astype(jnp.float32)).astype(jnp.bfloat16))

    chunk = NV // (row_count * col_count)
    virt = virtual_coeff.reshape(NBC, TB, NV)
    z = jnp.concatenate(
        [jnp.einsum("nwi,nwv->vi", h, virt, preferred_element_type=jnp.float32).astype(jnp.bfloat16) for h in halves],
        axis=1,
    )
    z = z.reshape(row_count, col_count, chunk, NOCC).transpose(1, 0, 2, 3)
    z = z.reshape(col_count * row_count * chunk, NOCC)
    w = lax.psum_scatter(z, "col", scatter_dimension=0, tiled=True).reshape(row_count, chunk, NOCC)

    got_rows = lax.all_to_all(w, "row", split_axis=0, concat_axis=0, tiled=True)
    out = got_rows.reshape(PB, 2, chunk, NOCC).transpose(2, 1, 0, 3)
    return out.reshape(chunk, AB * PB, NOCC)


def solution(mesh):
    in_specs = (
        P(("tensor", "row", "col"), None, None),
        P(("tensor", "row", "col"), None),
        P("col", None),
        P("row", None),
    )
    out_specs = P(("row", "col"), "tensor", None)
    return jax.shard_map(shards, mesh=mesh, in_specs=in_specs, out_specs=out_specs, check_vma=False)
```

```python
import jax
import jax.numpy as jnp
from jax import lax
from jax.sharding import PartitionSpec as P

TB = 64
PB = 8
AB = 2
MB = 2
NBC = 16
CAP = 2
NV = 2048
NOCC = 512


def shards(integral_tiles, tile_index, virtual_coeff, occupied_coeff):
    tensor_at = lax.axis_index("tensor")
    row_at = lax.axis_index("row")
    col_at = lax.axis_index("col")
    tensor_count = lax.axis_size("tensor")
    row_count = lax.axis_size("row")
    col_count = lax.axis_size("col")
    held = integral_tiles.shape[0]
    aux_blocks = tensor_count * AB
    mu_blocks = row_count * MB
    quarters = tensor_count * 2
    qsize = TB // quarters
    assert row_count == 2 * PB and tensor_count == 2 and quarters * qsize == TB

    owners = ("row", "tensor")
    dests = row_count * tensor_count
    lanes = qsize * TB
    send = integral_tiles.reshape(held, PB, quarters, lanes).transpose(1, 2, 0, 3).reshape(dests, held, lanes)
    local_index = jnp.stack(
        [tile_index[:, 0], tile_index[:, 1], tile_index[:, 2] - col_at * NBC], axis=1
    ).astype(jnp.bfloat16).reshape(1, 1, held * 3)
    index_row = jnp.pad(local_index, ((0, 0), (0, 0), (0, lanes - held * 3)))
    send = jnp.concatenate([send, jnp.broadcast_to(index_row, (dests, 1, lanes))], axis=1)
    recv = lax.all_to_all(send, owners, split_axis=0, concat_axis=0, tiled=True)
    slices = recv[:, :held, :].reshape(dests * held, lanes)
    index = recv[:, held, : held * 3].astype(jnp.int32).reshape(dests * held, 3)

    occ_all = lax.all_gather(occupied_coeff, "row", axis=0, tiled=True)
    quarter = 2 * (row_at % 2) + tensor_at
    occ_q = lax.dynamic_index_in_dim(
        occ_all.reshape(mu_blocks, quarters, qsize, NOCC), quarter, axis=1, keepdims=False
    ).reshape(mu_blocks * qsize, NOCC)

    block = (index[:, 0] * NBC + index[:, 2]) * mu_blocks + index[:, 1]
    blocks = aux_blocks * NBC * mu_blocks
    selector = (jnp.arange(blocks)[:, None] == block[None, :]).astype(jnp.bfloat16)
    dense = jnp.dot(selector, slices, preferred_element_type=jnp.float32).astype(jnp.bfloat16)
    dense = dense.reshape(aux_blocks * NBC, mu_blocks, qsize, TB).transpose(0, 3, 1, 2)
    dense = dense.reshape(aux_blocks * NBC, TB, mu_blocks * qsize)

    partial = jnp.einsum("bwk,ki->bwi", dense, occ_q, preferred_element_type=jnp.float32)
    partial = partial.reshape(aux_blocks, NBC, TB, NOCC)

    side = row_at % 2
    halves = []
    for half in jnp.split(partial.astype(jnp.bfloat16), 2, axis=3):
        pairs = half.reshape(tensor_count, AB, NBC, TB, NOCC // 2)
        mine = lax.dynamic_index_in_dim(pairs, tensor_at, axis=0, keepdims=False)
        other = lax.dynamic_index_in_dim(pairs, 1 - tensor_at, axis=0, keepdims=False)
        got_t = lax.ppermute(other, "tensor", perm=[(0, 1), (1, 0)])
        pair = (mine.astype(jnp.float32) + got_t.astype(jnp.float32)).astype(jnp.bfloat16)
        keep = lax.dynamic_index_in_dim(pair, side, axis=0, keepdims=False)
        give = lax.dynamic_index_in_dim(pair, 1 - side, axis=0, keepdims=False)
        got_r = lax.ppermute(give, "row", perm=[(i, i ^ 1) for i in range(row_count)])
        halves.append((keep.astype(jnp.float32) + got_r.astype(jnp.float32)).astype(jnp.bfloat16))

    chunk = NV // (row_count * col_count)
    virt = virtual_coeff.reshape(NBC, TB, NV)
    z = jnp.concatenate(
        [jnp.einsum("nwi,nwv->vi", h, virt, preferred_element_type=jnp.float32).astype(jnp.bfloat16) for h in halves],
        axis=1,
    )
    z = z.reshape(row_count, col_count, chunk, NOCC).transpose(1, 0, 2, 3)
    z = z.reshape(col_count * row_count * chunk, NOCC)
    w = lax.psum_scatter(z, "col", scatter_dimension=0, tiled=True).reshape(row_count, chunk, NOCC)

    side_count = 4
    by_x = [[g * side_count + k for k in range(side_count)] for g in range(row_count // side_count)]
    by_y = [[k * side_count + g for k in range(row_count // side_count)] for g in range(side_count)]
    w = w.reshape(row_count // side_count, side_count, chunk, NOCC)
    w = lax.all_to_all(w, "row", split_axis=1, concat_axis=1, axis_index_groups=by_x, tiled=True)
    w = lax.all_to_all(w, "row", split_axis=0, concat_axis=0, axis_index_groups=by_y, tiled=True)
    got_rows = w.reshape(row_count, chunk, NOCC)
    out = got_rows.reshape(PB, 2, chunk, NOCC).transpose(2, 1, 0, 3)
    return out.reshape(chunk, AB * PB, NOCC)


def solution(mesh):
    in_specs = (
        P(("tensor", "row", "col"), None, None),
        P(("tensor", "row", "col"), None),
        P("col", None),
        P("row", None),
    )
    out_specs = P(("row", "col"), "tensor", None)
    return jax.shard_map(shards, mesh=mesh, in_specs=in_specs, out_specs=out_specs, check_vma=False)
```

```python
import jax
import jax.numpy as jnp
from jax import lax
from jax.sharding import PartitionSpec as P

TB = 64
PB = 8
AB = 2
MB = 2
NBC = 16
CAP = 2
NV = 2048
NOCC = 512


def shards(integral_tiles, tile_index, virtual_coeff, occupied_coeff):
    tensor_at = lax.axis_index("tensor")
    row_at = lax.axis_index("row")
    col_at = lax.axis_index("col")
    tensor_count = lax.axis_size("tensor")
    row_count = lax.axis_size("row")
    col_count = lax.axis_size("col")
    held = integral_tiles.shape[0]
    aux_blocks = tensor_count * AB
    mu_blocks = row_count * MB
    quarters = tensor_count * 2
    qsize = TB // quarters
    assert row_count == 2 * PB and tensor_count == 2 and quarters * qsize == TB

    owners = ("row", "tensor")
    dests = row_count * tensor_count
    lanes = qsize * TB
    send = integral_tiles.reshape(held, PB, quarters, lanes).transpose(1, 2, 0, 3).reshape(dests, held, lanes)
    local_index = jnp.stack(
        [tile_index[:, 0], tile_index[:, 1], tile_index[:, 2] - col_at * NBC], axis=1
    ).astype(jnp.bfloat16).reshape(1, 1, held * 3)
    index_row = jnp.pad(local_index, ((0, 0), (0, 0), (0, lanes - held * 3)))
    send = jnp.concatenate([send, jnp.broadcast_to(index_row, (dests, 1, lanes))], axis=1)
    recv = lax.all_to_all(send, owners, split_axis=0, concat_axis=0, tiled=True)
    slices = recv[:, :held, :].reshape(dests * held, lanes)
    index = recv[:, held, : held * 3].astype(jnp.int32).reshape(dests * held, 3)

    occ_local = occupied_coeff.reshape(MB, 2, tensor_count, qsize, NOCC)
    occ_local = lax.dynamic_index_in_dim(occ_local, tensor_at, axis=2, keepdims=False)
    occ_half = lax.all_gather(occ_local, "row", axis=0, tiled=True)
    pick = row_at % 2 + jnp.minimum(index[0, 0], 0)
    occ_q = lax.dynamic_index_in_dim(occ_half, pick, axis=1, keepdims=False).reshape(mu_blocks * qsize, NOCC)

    block = (index[:, 0] * NBC + index[:, 2]) * mu_blocks + index[:, 1]
    blocks = aux_blocks * NBC * mu_blocks
    selector = (jnp.arange(blocks)[:, None] == block[None, :]).astype(jnp.bfloat16)
    dense = jnp.dot(selector, slices, preferred_element_type=jnp.float32).astype(jnp.bfloat16)
    dense = dense.reshape(aux_blocks * NBC, mu_blocks, qsize, TB).transpose(0, 3, 1, 2)
    dense = dense.reshape(aux_blocks * NBC, TB, mu_blocks * qsize)


    side = row_at % 2
    halves = []
    for occ_h in jnp.split(occ_q, 2, axis=1):
        half = jnp.einsum("bwk,ki->bwi", dense, occ_h, preferred_element_type=jnp.float32)
        pairs = half.astype(jnp.bfloat16).reshape(tensor_count, AB, NBC, TB, NOCC // 2)
        mine = lax.dynamic_index_in_dim(pairs, tensor_at, axis=0, keepdims=False)
        other = lax.dynamic_index_in_dim(pairs, 1 - tensor_at, axis=0, keepdims=False)
        got_t = lax.ppermute(other, "tensor", perm=[(0, 1), (1, 0)])
        pair = (mine.astype(jnp.float32) + got_t.astype(jnp.float32)).astype(jnp.bfloat16)
        keep = lax.dynamic_index_in_dim(pair, side, axis=0, keepdims=False)
        give = lax.dynamic_index_in_dim(pair, 1 - side, axis=0, keepdims=False)
        got_r = lax.ppermute(give, "row", perm=[(i, i ^ 1) for i in range(row_count)])
        halves.append((keep.astype(jnp.float32) + got_r.astype(jnp.float32)).astype(jnp.bfloat16))

    chunk = NV // (row_count * col_count)
    virt = virtual_coeff.reshape(NBC, TB, NV)
    z = jnp.concatenate(
        [jnp.einsum("nwi,nwv->vi", h, virt, preferred_element_type=jnp.float32).astype(jnp.bfloat16) for h in halves],
        axis=1,
    )
    z = z.reshape(row_count, col_count, chunk, NOCC).transpose(1, 0, 2, 3)
    z = z.reshape(col_count * row_count * chunk, NOCC)
    w = lax.psum_scatter(z, "col", scatter_dimension=0, tiled=True).reshape(row_count, chunk, NOCC)

    got_rows = lax.all_to_all(w, "row", split_axis=0, concat_axis=0, tiled=True)
    out = got_rows.reshape(PB, 2, chunk, NOCC).transpose(2, 1, 0, 3)
    return out.reshape(chunk, AB * PB, NOCC)


def solution(mesh):
    in_specs = (
        P(("tensor", "row", "col"), None, None),
        P(("tensor", "row", "col"), None),
        P("col", None),
        P("row", None),
    )
    out_specs = P(("row", "col"), "tensor", None)
    return jax.shard_map(shards, mesh=mesh, in_specs=in_specs, out_specs=out_specs, check_vma=False)
```

```python
import jax
import jax.numpy as jnp
from jax import lax
from jax.sharding import PartitionSpec as P

TB = 64
PB = 8
AB = 2
MB = 2
NBC = 16
CAP = 2
NV = 2048
NOCC = 512


def shards(integral_tiles, tile_index, virtual_coeff, occupied_coeff):
    tensor_at = lax.axis_index("tensor")
    row_at = lax.axis_index("row")
    col_at = lax.axis_index("col")
    tensor_count = lax.axis_size("tensor")
    row_count = lax.axis_size("row")
    col_count = lax.axis_size("col")
    held = integral_tiles.shape[0]
    aux_blocks = tensor_count * AB
    mu_blocks = row_count * MB
    quarters = tensor_count * 2
    qsize = TB // quarters
    assert row_count == 2 * PB and tensor_count == 2 and quarters * qsize == TB

    owners = ("row", "tensor")
    dests = row_count * tensor_count
    lanes = qsize * TB
    send = integral_tiles.reshape(held, PB, quarters, lanes).transpose(1, 2, 0, 3).reshape(dests, held, lanes)
    local_index = jnp.stack(
        [tile_index[:, 0], tile_index[:, 1], tile_index[:, 2] - col_at * NBC], axis=1
    ).astype(jnp.bfloat16).reshape(1, 1, held * 3)
    index_row = jnp.pad(local_index, ((0, 0), (0, 0), (0, lanes - held * 3)))
    send = jnp.concatenate([send, jnp.broadcast_to(index_row, (dests, 1, lanes))], axis=1)
    recv = lax.all_to_all(send, owners, split_axis=0, concat_axis=0, tiled=True)
    slices = recv[:, :held, :].reshape(dests * held, lanes)
    index = recv[:, held, : held * 3].astype(jnp.int32).reshape(dests * held, 3)

    occ_all = lax.all_gather(occupied_coeff, "row", axis=0, tiled=True)
    quarter = 2 * (row_at % 2) + tensor_at
    occ_q = lax.dynamic_index_in_dim(
        occ_all.reshape(mu_blocks, quarters, qsize, NOCC), quarter, axis=1, keepdims=False
    ).reshape(mu_blocks * qsize, NOCC)

    block = (index[:, 0] * NBC + index[:, 2]) * mu_blocks + index[:, 1]
    blocks = aux_blocks * NBC * mu_blocks
    selector = (jnp.arange(blocks)[:, None] == block[None, :]).astype(jnp.bfloat16)
    dense = jnp.dot(selector, slices, preferred_element_type=jnp.float32).astype(jnp.bfloat16)
    dense = dense.reshape(aux_blocks * NBC, mu_blocks, qsize, TB).transpose(0, 3, 1, 2)
    dense = dense.reshape(aux_blocks * NBC, TB, mu_blocks * qsize)

    partial = jnp.einsum("bwk,ki->bwi", dense, occ_q, preferred_element_type=jnp.float32)
    partial = partial.reshape(aux_blocks, NBC, TB, NOCC)

    side = row_at % 2
    halves = []
    pieces = 4
    for half in jnp.split(partial.astype(jnp.bfloat16), pieces, axis=3):
        pairs = half.reshape(tensor_count, AB, NBC, TB, NOCC // pieces)
        mine = lax.dynamic_index_in_dim(pairs, tensor_at, axis=0, keepdims=False)
        other = lax.dynamic_index_in_dim(pairs, 1 - tensor_at, axis=0, keepdims=False)
        got_t = lax.ppermute(other, "tensor", perm=[(0, 1), (1, 0)])
        pair = (mine.astype(jnp.float32) + got_t.astype(jnp.float32)).astype(jnp.bfloat16)
        keep = lax.dynamic_index_in_dim(pair, side, axis=0, keepdims=False)
        give = lax.dynamic_index_in_dim(pair, 1 - side, axis=0, keepdims=False)
        got_r = lax.ppermute(give, "row", perm=[(i, i ^ 1) for i in range(row_count)])
        halves.append((keep.astype(jnp.float32) + got_r.astype(jnp.float32)).astype(jnp.bfloat16))

    chunk = NV // (row_count * col_count)
    virt = virtual_coeff.reshape(NBC, TB, NV)
    z = jnp.concatenate(
        [jnp.einsum("nwi,nwv->vi", h, virt, preferred_element_type=jnp.float32).astype(jnp.bfloat16) for h in halves],
        axis=1,
    )
    z = z.reshape(row_count, col_count, chunk, NOCC).transpose(1, 0, 2, 3)
    z = z.reshape(col_count * row_count * chunk, NOCC)
    w = lax.psum_scatter(z, "col", scatter_dimension=0, tiled=True).reshape(row_count, chunk, NOCC)

    got_rows = lax.all_to_all(w, "row", split_axis=0, concat_axis=0, tiled=True)
    out = got_rows.reshape(PB, 2, chunk, NOCC).transpose(2, 1, 0, 3)
    return out.reshape(chunk, AB * PB, NOCC)


def solution(mesh):
    in_specs = (
        P(("tensor", "row", "col"), None, None),
        P(("tensor", "row", "col"), None),
        P("col", None),
        P("row", None),
    )
    out_specs = P(("row", "col"), "tensor", None)
    return jax.shard_map(shards, mesh=mesh, in_specs=in_specs, out_specs=out_specs, check_vma=False)
```

```python
import jax
import jax.numpy as jnp
from jax import lax
from jax.sharding import PartitionSpec as P

TB = 64
PB = 8
AB = 2
MB = 2
NBC = 16
CAP = 2
NV = 2048
NOCC = 512


def shards(integral_tiles, tile_index, virtual_coeff, occupied_coeff):
    tensor_at = lax.axis_index("tensor")
    row_at = lax.axis_index("row")
    col_at = lax.axis_index("col")
    tensor_count = lax.axis_size("tensor")
    row_count = lax.axis_size("row")
    col_count = lax.axis_size("col")
    held = integral_tiles.shape[0]
    aux_blocks = tensor_count * AB
    mu_blocks = row_count * MB
    quarters = tensor_count * 2
    qsize = TB // quarters
    assert row_count == 2 * PB and tensor_count == 2 and quarters * qsize == TB

    owners = ("row", "tensor")
    dests = row_count * tensor_count
    lanes = qsize * TB
    send = integral_tiles.reshape(held, PB, quarters, lanes).transpose(1, 2, 0, 3).reshape(dests, held, lanes)
    local_index = jnp.stack(
        [tile_index[:, 0], tile_index[:, 1], tile_index[:, 2] - col_at * NBC], axis=1
    ).astype(jnp.bfloat16).reshape(1, 1, held * 3)
    index_row = jnp.pad(local_index, ((0, 0), (0, 0), (0, lanes - held * 3)))
    send = jnp.concatenate([send, jnp.broadcast_to(index_row, (dests, 1, lanes))], axis=1)
    recv = lax.all_to_all(send, owners, split_axis=0, concat_axis=0, tiled=True)
    slices = recv[:, :held, :].reshape(dests * held, lanes)
    index = recv[:, held, : held * 3].astype(jnp.int32).reshape(dests * held, 3)

    occ_all = lax.all_gather(occupied_coeff, "row", axis=0, tiled=True)
    quarter = 2 * (row_at % 2) + tensor_at
    occ_q = lax.dynamic_index_in_dim(
        occ_all.reshape(mu_blocks, quarters, qsize, NOCC), quarter, axis=1, keepdims=False
    ).reshape(mu_blocks * qsize, NOCC)

    block = (index[:, 0] * NBC + index[:, 2]) * mu_blocks + index[:, 1]
    blocks = aux_blocks * NBC * mu_blocks
    selector = (jnp.arange(blocks)[:, None] == block[None, :]).astype(jnp.bfloat16)
    dense = jnp.dot(selector, slices, preferred_element_type=jnp.float32).astype(jnp.bfloat16)
    dense = dense.reshape(aux_blocks * NBC, mu_blocks, qsize, TB).transpose(0, 3, 1, 2)
    dense = dense.reshape(aux_blocks * NBC, TB, mu_blocks * qsize)

    partial = jnp.einsum("bwk,ki->bwi", dense, occ_q, preferred_element_type=jnp.float32)
    partial = partial.reshape(aux_blocks, NBC, TB, NOCC)

    side = row_at % 2
    halves = []
    for half in jnp.split(partial.astype(jnp.bfloat16), 2, axis=3):
        pairs = half.reshape(tensor_count, AB, NBC, TB, NOCC // 2)
        mine = lax.dynamic_index_in_dim(pairs, tensor_at, axis=0, keepdims=False)
        other = lax.dynamic_index_in_dim(pairs, 1 - tensor_at, axis=0, keepdims=False)
        got_t = lax.ppermute(other, "tensor", perm=[(0, 1), (1, 0)])
        pair = (mine.astype(jnp.float32) + got_t.astype(jnp.float32)).astype(jnp.bfloat16)
        keep = lax.dynamic_index_in_dim(pair, side, axis=0, keepdims=False)
        give = lax.dynamic_index_in_dim(pair, 1 - side, axis=0, keepdims=False)
        got_r = lax.ppermute(give, "row", perm=[(i, i ^ 1) for i in range(row_count)])
        halves.append((keep.astype(jnp.float32) + got_r.astype(jnp.float32)).astype(jnp.bfloat16))

    chunk = NV // (row_count * col_count)
    virt = virtual_coeff.reshape(NBC, TB, NV)
    z = jnp.concatenate(
        [jnp.einsum("nwi,nwv->vi", h, virt, preferred_element_type=jnp.float32).astype(jnp.bfloat16) for h in halves],
        axis=1,
    )
    z = z.reshape(row_count, col_count, chunk, NOCC).transpose(1, 0, 2, 3)
    z = z.reshape(col_count * row_count * chunk, NOCC)
    w = lax.psum_scatter(z, "col", scatter_dimension=0, tiled=True).reshape(row_count, chunk, NOCC)

    arrived = [lax.dynamic_index_in_dim(w, row_at, axis=0, keepdims=False)]
    for shift in range(1, row_count):
        piece = lax.dynamic_index_in_dim(w, (row_at + shift) % row_count, axis=0, keepdims=False)
        perm = [(i, (i + shift) % row_count) for i in range(row_count)]
        arrived.append(lax.ppermute(piece, "row", perm=perm))
    got_rows = jnp.stack(arrived)[(row_at - jnp.arange(row_count)) % row_count]
    out = got_rows.reshape(PB, 2, chunk, NOCC).transpose(2, 1, 0, 3)
    return out.reshape(chunk, AB * PB, NOCC)


def solution(mesh):
    in_specs = (
        P(("tensor", "row", "col"), None, None),
        P(("tensor", "row", "col"), None),
        P("col", None),
        P("row", None),
    )
    out_specs = P(("row", "col"), "tensor", None)
    return jax.shard_map(shards, mesh=mesh, in_specs=in_specs, out_specs=out_specs, check_vma=False)
```

```python
import jax
import jax.numpy as jnp
from jax import lax
from jax.sharding import PartitionSpec as P

TB = 64
PB = 8
AB = 2
MB = 2
NBC = 16
CAP = 2
NV = 2048
NOCC = 512


def shards(integral_tiles, tile_index, virtual_coeff, occupied_coeff):
    tensor_at = lax.axis_index("tensor")
    row_at = lax.axis_index("row")
    col_at = lax.axis_index("col")
    tensor_count = lax.axis_size("tensor")
    row_count = lax.axis_size("row")
    col_count = lax.axis_size("col")
    held = integral_tiles.shape[0]
    aux_blocks = tensor_count * AB
    mu_blocks = row_count * MB
    quarters = tensor_count * 2
    qsize = TB // quarters
    assert row_count == 2 * PB and tensor_count == 2 and quarters * qsize == TB

    owners = ("row", "tensor")
    dests = row_count * tensor_count
    lanes = qsize * TB
    send = integral_tiles.reshape(held, PB, quarters, lanes).transpose(1, 2, 0, 3).reshape(dests, held, lanes)
    local_index = jnp.stack(
        [tile_index[:, 0], tile_index[:, 1], tile_index[:, 2] - col_at * NBC], axis=1
    ).astype(jnp.bfloat16).reshape(1, 1, held * 3)
    index_row = jnp.pad(local_index, ((0, 0), (0, 0), (0, lanes - held * 3)))
    send = jnp.concatenate([send, jnp.broadcast_to(index_row, (dests, 1, lanes))], axis=1)
    recv = lax.all_to_all(send, owners, split_axis=0, concat_axis=0, tiled=True)
    slices = recv[:, :held, :].reshape(dests * held, lanes)
    index = recv[:, held, : held * 3].astype(jnp.int32).reshape(dests * held, 3)

    occ_all = lax.all_gather(occupied_coeff, "row", axis=0, tiled=True)
    quarter = 2 * (row_at % 2) + tensor_at
    occ_q = lax.dynamic_index_in_dim(
        occ_all.reshape(mu_blocks, quarters, qsize, NOCC), quarter, axis=1, keepdims=False
    ).reshape(mu_blocks * qsize, NOCC)

    block = (index[:, 0] * NBC + index[:, 2]) * mu_blocks + index[:, 1]
    blocks = aux_blocks * NBC * mu_blocks
    selector = (jnp.arange(blocks)[:, None] == block[None, :]).astype(jnp.bfloat16)
    dense = jnp.dot(selector, slices, preferred_element_type=jnp.float32).astype(jnp.bfloat16)
    dense = dense.reshape(aux_blocks * NBC, mu_blocks, qsize, TB).transpose(0, 3, 1, 2)
    dense = dense.reshape(aux_blocks * NBC, TB, mu_blocks * qsize)

    partial = jnp.einsum("bwk,ki->bwi", dense, occ_q, preferred_element_type=jnp.float32)
    partial = partial.reshape(aux_blocks, NBC, TB, NOCC)

    side = row_at % 2
    halves = []
    for half in jnp.split(partial.astype(jnp.bfloat16), 2, axis=3):
        pairs = half.reshape(tensor_count, AB, NBC, TB, NOCC // 2)
        mine = lax.dynamic_index_in_dim(pairs, tensor_at, axis=0, keepdims=False)
        other = lax.dynamic_index_in_dim(pairs, 1 - tensor_at, axis=0, keepdims=False)
        got_t = lax.ppermute(other, "tensor", perm=[(0, 1), (1, 0)])
        pair = (mine.astype(jnp.float32) + got_t.astype(jnp.float32)).astype(jnp.bfloat16)
        keep = lax.dynamic_index_in_dim(pair, side, axis=0, keepdims=False)
        give = lax.dynamic_index_in_dim(pair, 1 - side, axis=0, keepdims=False)
        got_r = lax.ppermute(give, "row", perm=[(i, i ^ 1) for i in range(row_count)])
        halves.append((keep.astype(jnp.float32) + got_r.astype(jnp.float32)).astype(jnp.bfloat16))

    chunk = NV // (row_count * col_count)
    virt = virtual_coeff.reshape(NBC, TB, NV)
    z = jnp.concatenate(
        [
            jnp.einsum("nwi,nwv->vi", h, virt, preferred_element_type=jnp.float32)
            .astype(jnp.bfloat16)
            .reshape(row_count, col_count, chunk, NOCC // 2)
            .transpose(1, 0, 2, 3)
            for h in halves
        ],
        axis=3,
    )
    z = z.reshape(col_count * row_count * chunk, NOCC)
    w = lax.psum_scatter(z, "col", scatter_dimension=0, tiled=True).reshape(row_count, chunk, NOCC)

    got_rows = lax.all_to_all(w, "row", split_axis=0, concat_axis=0, tiled=True)
    out = got_rows.reshape(PB, 2, chunk, NOCC).transpose(2, 1, 0, 3)
    return out.reshape(chunk, AB * PB, NOCC)


def solution(mesh):
    in_specs = (
        P(("tensor", "row", "col"), None, None),
        P(("tensor", "row", "col"), None),
        P("col", None),
        P("row", None),
    )
    out_specs = P(("row", "col"), "tensor", None)
    return jax.shard_map(shards, mesh=mesh, in_specs=in_specs, out_specs=out_specs, check_vma=False)
```
